32 devices in a mesh: grp: 2 (over y), row: 4 (over z), col: 4 (over x, core).
Axes of the slice: x: 2, y: 2, z: 4, core: 2. Of those that a mesh axis runs over, the one named last changes fastest.
Arguments:
- tokens: bfloat16 [256, 10240], P(('grp', 'col'), 'row'), parts along dimension 0, may hold values from -6 to 6
- gate_up: bfloat16 [2, 10240, 26624], P(None, 'row', 'col'), may hold values from -0.0625 to 0.0625
Outputs:
- hidden: bfloat16 [256, 26624], P(('grp', 'row'), 'col'), parts along dimension 0
The draws below stay inside these ranges and needn't reach their ends.
There are 2 independent parts, one for each index of `grp`. The reference program is written for one: setup_inputs(seed, part) draws one part's arguments, and reference() takes and returns one part's arrays. A program takes and returns all parts, laid end to end along the dimension named above; an argument that names none is the same for every part. Nothing has to cross between parts.
All inputs are finite; a program needn't handle non-finite values.
Results may differ from the reference program's by a relative error of at most 0.015.
Values may be sent and summed in bfloat16 or wider, within the bound.
No kernel may reach another device: no remote copies, remote signals or barrier semaphores. Data moves between devices by JAX's collectives and lax.ppermute only.
A program may use at most 192 MiB of HBM per device.

```python
import jax
import jax.numpy as jnp
from jax import lax

D = 10240
FF = 26624
ROW_BLOCKS = 4
TOKENS = 128


def spiked(values, key, source, target, shards_of, factor):
    def block_of(axis_at):
        return (jnp.arange(values.shape[axis_at]) // (values.shape[axis_at] // shards_of)).reshape((-1,) + (1,) * (values.ndim - 1 - axis_at))

    first = jax.random.permutation(key, shards_of)[block_of(target)]
    second = (block_of(target) + shards_of // 2) % shards_of
    return jnp.where((block_of(source) == first) | (block_of(source) == second), factor * values, values)


def block_levels(rng, extent, cuts, least, top_value):
    def one(position, parts):
        draws = jax.random.uniform(jax.random.fold_in(jax.random.fold_in(rng, 6), position), (parts,), jnp.float32, least / len(cuts), top_value / len(cuts))
        return jnp.repeat(jnp.exp(draws), extent[position] // parts).reshape((-1,) + (1,) * (len(extent) - position - 1))

    level = one(*cuts[0])
    for cut in cuts[1:]:
        level = level * one(*cut)
    return level


def scatter_about(own_key, shape, scale, most, cuts=(), kind=jnp.bfloat16):
    array = jax.random.normal(own_key, shape, jnp.float32) * scale
    if len(cuts) > 0:
        array = block_levels(own_key, shape, cuts, -0.22, 0.18) * array
    return jnp.clip(array, min=-most, max=most).astype(kind)


def heavy_noise(stream_key, shape, scale, limit, split, heavy, kind=jnp.bfloat16):
    result = scale * jax.random.normal(stream_key, shape, jnp.float32)
    if split:
        result = result * block_levels(stream_key, shape, split, -0.22, 0.18)
    return jnp.clip(spiked(result, jax.random.fold_in(stream_key, 3), *heavy), -limit, limit).astype(kind)


def setup_inputs(seed: int = 0, part: int = 0) -> dict:
    splits = jax.random.split(jax.random.key(seed), 3)
    part_splits = jax.random.split(jax.random.fold_in(splits[2], part), 3)
    return {
        "tokens": heavy_noise(part_splits[0], (TOKENS, D), 1.0, 6.0, ((0, 4), (1, 4)), (1, 0, 4, 2.0)),
        "gate_up": scatter_about(splits[1], (2, D, FF), D ** -0.5, 0.0625, ((1, 4), (2, 4))),
    }


def reference(tokens, gate_up):
    width = D // ROW_BLOCKS

    def add_block(total, index):
        start = (index * width).astype(jnp.int32)
        rows = lax.dynamic_slice_in_dim(tokens, start, width, 1).astype(jnp.float32)
        weights = lax.dynamic_slice_in_dim(gate_up, start, width, 1).astype(jnp.float32)
        part = jnp.einsum("td,gdf->gtf", rows, weights).astype(jnp.bfloat16)
        part = lax.optimization_barrier(part)
        return total + part.astype(jnp.float32), None

    empty = jnp.zeros((2, tokens.shape[0], gate_up.shape[2]), jnp.float32)
    proj, unused = lax.scan(add_block, empty, jnp.arange(ROW_BLOCKS, dtype=jnp.int32))
    return (jax.nn.silu(proj[0]) * proj[1]).astype(jnp.bfloat16)
```

```python
import jax
import jax.numpy as jnp
from jax import lax
from jax.sharding import PartitionSpec as P

CHUNKS = 4


def gather_cols(tokens, m):
    c = lax.axis_index("col")
    rows = tokens.shape[0]
    buf = jnp.zeros((m, rows, tokens.shape[1]), tokens.dtype)
    buf = lax.dynamic_update_index_in_dim(buf, tokens, c, 0)
    for s in range(1, m):
        got = lax.ppermute(tokens, "col", [(i, (i + s) % m) for i in range(m)])
        buf = lax.dynamic_update_index_in_dim(buf, got, (c - s + m) % m, 0)
    return buf.reshape(m * rows, tokens.shape[1])


def line_reduce(part, n, p):
    def block(d):
        return lax.dynamic_index_in_dim(part, jnp.clip(d, 0, n - 1), 0, keepdims=False)

    def add(a, b):
        return (a.astype(jnp.float32) + b.astype(jnp.float32)).astype(jnp.bfloat16)

    with jax.named_scope("up"):
        origin = [lax.ppermute(part[n - r], "row", [(0, 1)]) for r in range(1, n)]
        plus = origin[0]
        for r in range(2, n):
            sent = lax.ppermute(add(block(p + n - r), plus), "row", [(q, q + 1) for q in range(1, r)])
            plus = origin[r - 1] + sent
    with jax.named_scope("down"):
        origin = [lax.ppermute(part[r - 1], "row", [(n - 1, n - 2)]) for r in range(1, n)]
        minus = origin[0]
        for r in range(2, n):
            sent = lax.ppermute(add(block(p - n + r), minus), "row", [(q, q - 1) for q in range(n - r, n - 1)])
            minus = origin[r - 1] + sent
    return plus, minus


def on_device(tokens, gate_up, n, m):
    p = lax.axis_index("row")
    gathered = gather_cols(tokens, m)
    t = gathered.shape[0]
    tb = t // n
    f = gate_up.shape[2]
    units = f // 128
    k = min(CHUNKS, units)
    edges = [128 * (units * i // k) for i in range(k + 1)]
    edges[-1] = f
    outs = []
    for i in range(k):
        w = gate_up[:, :, edges[i] : edges[i + 1]]
        part = jnp.einsum("td,gdf->tgf", gathered, w, preferred_element_type=jnp.float32).astype(jnp.bfloat16)
        part = part.reshape(n, tb, 2, edges[i + 1] - edges[i])
        own = lax.dynamic_index_in_dim(part, p, 0, keepdims=False).astype(jnp.float32)
        if n > 1:
            plus, minus = line_reduce(part, n, p)
            own = own + plus.astype(jnp.float32) + minus.astype(jnp.float32)
        outs.append((jax.nn.silu(own[:, 0]) * own[:, 1]).astype(jnp.bfloat16))
    return jnp.concatenate(outs, axis=1)


def solution(mesh):
    n = mesh.shape["row"]
    m = mesh.shape["col"]
    placed = (P(("grp", "col"), "row"), P(None, "row", "col"))

    def body(tokens, gate_up):
        return on_device(tokens, gate_up, n, m)

    return jax.shard_map(
        body, mesh=mesh, in_specs=placed, out_specs=P(("grp", "row"), "col"), check_vma=False
    )
```

```python
import jax
import jax.numpy as jnp
from jax import lax
from jax.sharding import PartitionSpec as P

CHUNKS = 4


def gather_cols(tokens, m):
    c = lax.axis_index("col")
    rows = tokens.shape[0]
    buf = jnp.zeros((m, rows, tokens.shape[1]), tokens.dtype)
    buf = lax.dynamic_update_index_in_dim(buf, tokens, c, 0)
    for s in range(1, m):
        got = lax.ppermute(tokens, "col", [(i, (i + s) % m) for i in range(m)])
        buf = lax.dynamic_update_index_in_dim(buf, got, (c - s + m) % m, 0)
    return buf.reshape(m * rows, tokens.shape[1])


def line_reduce(part, n, p):
    def block(d):
        return lax.dynamic_index_in_dim(part, jnp.clip(d, 0, n - 1), 0, keepdims=False)

    def add(a, b):
        return (a.astype(jnp.float32) + b.astype(jnp.float32)).astype(jnp.bfloat16)

    with jax.named_scope("up"):
        origin = [lax.ppermute(part[n - r], "row", [(0, 1)]) for r in range(1, n)]
        plus = origin[0]
        for r in range(2, n):
            sent = lax.ppermute(add(block(p + n - r), plus), "row", [(q, q + 1) for q in range(1, r)])
            plus = origin[r - 1] + sent
    with jax.named_scope("down"):
        origin = [lax.ppermute(part[r - 1], "row", [(n - 1, n - 2)]) for r in range(1, n)]
        minus = origin[0]
        for r in range(2, n):
            sent = lax.ppermute(add(block(p - n + r), minus), "row", [(q, q - 1) for q in range(n - r, n - 1)])
            minus = origin[r - 1] + sent
    return plus, minus


def on_device(tokens, gate_up, n, m):
    p = lax.axis_index("row")
    gathered = lax.all_gather(tokens, "col", axis=0, tiled=True)
    t = gathered.shape[0]
    tb = t // n
    f = gate_up.shape[2]
    units = f // 128
    k = min(CHUNKS, units)
    edges = [128 * (units * i // k) for i in range(k + 1)]
    edges[-1] = f
    outs = []
    for i in range(k):
        w = gate_up[:, :, edges[i] : edges[i + 1]]
        part = jnp.einsum("td,gdf->tgf", gathered, w, preferred_element_type=jnp.float32).astype(jnp.bfloat16)
        own = lax.psum_scatter(part, "row", scatter_dimension=0, tiled=True).astype(jnp.float32)
        outs.append((jax.nn.silu(own[:, 0]) * own[:, 1]).astype(jnp.bfloat16))
    return jnp.concatenate(outs, axis=1)


def solution(mesh):
    n = mesh.shape["row"]
    m = mesh.shape["col"]
    placed = (P(("grp", "col"), "row"), P(None, "row", "col"))

    def body(tokens, gate_up):
        return on_device(tokens, gate_up, n, m)

    return jax.shard_map(
        body, mesh=mesh, in_specs=placed, out_specs=P(("grp", "row"), "col"), check_vma=False
    )
```

```python
import jax
import jax.numpy as jnp
from jax import lax
from jax.sharding import PartitionSpec as P

CHUNKS = 1


def gather_cols(tokens, m):
    c = lax.axis_index("col")
    rows = tokens.shape[0]
    buf = jnp.zeros((m, rows, tokens.shape[1]), tokens.dtype)
    buf = lax.dynamic_update_index_in_dim(buf, tokens, c, 0)
    for s in range(1, m):
        got = lax.ppermute(tokens, "col", [(i, (i + s) % m) for i in range(m)])
        buf = lax.dynamic_update_index_in_dim(buf, got, (c - s + m) % m, 0)
    return buf.reshape(m * rows, tokens.shape[1])


def line_reduce(part, n, p):
    def block(d):
        return lax.dynamic_index_in_dim(part, jnp.clip(d, 0, n - 1), 0, keepdims=False)

    def add(a, b):
        return (a.astype(jnp.float32) + b.astype(jnp.float32)).astype(jnp.bfloat16)

    with jax.named_scope("up"):
        origin = [lax.ppermute(part[n - r], "row", [(0, 1)]) for r in range(1, n)]
        plus = origin[0]
        for r in range(2, n):
            sent = lax.ppermute(add(block(p + n - r), plus), "row", [(q, q + 1) for q in range(1, r)])
            plus = origin[r - 1] + sent
    with jax.named_scope("down"):
        origin = [lax.ppermute(part[r - 1], "row", [(n - 1, n - 2)]) for r in range(1, n)]
        minus = origin[0]
        for r in range(2, n):
            sent = lax.ppermute(add(block(p - n + r), minus), "row", [(q, q - 1) for q in range(n - r, n - 1)])
            minus = origin[r - 1] + sent
    return plus, minus


def on_device(tokens, gate_up, n, m):
    p = lax.axis_index("row")
    gathered = gather_cols(tokens, m)
    t = gathered.shape[0]
    tb = t // n
    f = gate_up.shape[2]
    units = f // 128
    k = min(CHUNKS, units)
    edges = [128 * (units * i // k) for i in range(k + 1)]
    edges[-1] = f
    outs = []
    for i in range(k):
        w = gate_up[:, :, edges[i] : edges[i + 1]]
        part = jnp.einsum("td,gdf->tgf", gathered, w, preferred_element_type=jnp.float32).astype(jnp.bfloat16)
        part = part.reshape(n, tb, 2, edges[i + 1] - edges[i])
        own = lax.dynamic_index_in_dim(part, p, 0, keepdims=False).astype(jnp.float32)
        if n > 1:
            plus, minus = line_reduce(part, n, p)
            own = own + plus.astype(jnp.float32) + minus.astype(jnp.float32)
        outs.append((jax.nn.silu(own[:, 0]) * own[:, 1]).astype(jnp.bfloat16))
    return jnp.concatenate(outs, axis=1)


def solution(mesh):
    n = mesh.shape["row"]
    m = mesh.shape["col"]
    placed = (P(("grp", "col"), "row"), P(None, "row", "col"))

    def body(tokens, gate_up):
        return on_device(tokens, gate_up, n, m)

    return jax.shard_map(
        body, mesh=mesh, in_specs=placed, out_specs=P(("grp", "row"), "col"), check_vma=False
    )
```

```python
import jax
import jax.numpy as jnp
from jax import lax
from jax.sharding import PartitionSpec as P

CHUNKS = 2


def gather_cols(tokens, m):
    c = lax.axis_index("col")
    rows = tokens.shape[0]
    buf = jnp.zeros((m, rows, tokens.shape[1]), tokens.dtype)
    buf = lax.dynamic_update_index_in_dim(buf, tokens, c, 0)
    for s in range(1, m):
        got = lax.ppermute(tokens, "col", [(i, (i + s) % m) for i in range(m)])
        buf = lax.dynamic_update_index_in_dim(buf, got, (c - s + m) % m, 0)
    return buf.reshape(m * rows, tokens.shape[1])


def line_reduce(part, n, p):
    def block(d):
        return lax.dynamic_index_in_dim(part, jnp.clip(d, 0, n - 1), 0, keepdims=False)

    def add(a, b):
        return (a.astype(jnp.float32) + b.astype(jnp.float32)).astype(jnp.bfloat16)

    with jax.named_scope("up"):
        origin = [lax.ppermute(part[n - r], "row", [(0, 1)]) for r in range(1, n)]
        first = origin[0]
        plus = origin[0]
        for r in range(2, n):
            sent = lax.ppermute(add(block(p + n - r), plus), "row", [(q, q + 1) for q in range(1, r)])
            plus = origin[r - 1] + sent
    with jax.named_scope("down"):
        origin = [lax.ppermute(part[r - 1], "row", [(n - 1, n - 2)]) for r in range(1, n)]
        minus = origin[0]
        for r in range(2, n):
            sent = lax.ppermute(add(block(p - n + r), minus), "row", [(q, q - 1) for q in range(n - r, n - 1)])
            minus = origin[r - 1] + sent
    return plus, minus, (first, origin[0])


def on_device(tokens, gate_up, n, m):
    p = lax.axis_index("row")
    gathered = gather_cols(tokens, m)
    t = gathered.shape[0]
    tb = t // n
    f = gate_up.shape[2]
    units = f // 128
    k = min(CHUNKS, units)
    edges = [128 * (units * i // k) for i in range(k + 1)]
    edges[-1] = f
    outs = []
    held = gathered
    for i in range(k):
        w = gate_up[:, :, edges[i] : edges[i + 1]]
        part = jnp.einsum("td,gdf->tgf", held, w, preferred_element_type=jnp.float32).astype(jnp.bfloat16)
        part = part.reshape(n, tb, 2, edges[i + 1] - edges[i])
        own = lax.dynamic_index_in_dim(part, p, 0, keepdims=False).astype(jnp.float32)
        if n > 1:
            plus, minus, first = line_reduce(part, n, p)
            held = lax.optimization_barrier((gathered, first))[0]
            own = own + plus.astype(jnp.float32) + minus.astype(jnp.float32)
        outs.append((jax.nn.silu(own[:, 0]) * own[:, 1]).astype(jnp.bfloat16))
    return jnp.concatenate(outs, axis=1)


def solution(mesh):
    n = mesh.shape["row"]
    m = mesh.shape["col"]
    placed = (P(("grp", "col"), "row"), P(None, "row", "col"))

    def body(tokens, gate_up):
        return on_device(tokens, gate_up, n, m)

    return jax.shard_map(
        body, mesh=mesh, in_specs=placed, out_specs=P(("grp", "row"), "col"), check_vma=False
    )
```

```python
import jax
import jax.numpy as jnp
from jax import lax
from jax.sharding import PartitionSpec as P

CHUNKS = 2


def gather_cols(tokens, m):
    c = lax.axis_index("col")
    rows = tokens.shape[0]
    buf = jnp.zeros((m, rows, tokens.shape[1]), tokens.dtype)
    buf = lax.dynamic_update_index_in_dim(buf, tokens, c, 0)
    for s in range(1, m):
        got = lax.ppermute(tokens, "col", [(i, (i + s) % m) for i in range(m)])
        buf = lax.dynamic_update_index_in_dim(buf, got, (c - s + m) % m, 0)
    return buf.reshape(m * rows, tokens.shape[1])


def line_reduce(part, n, p):
    def block(d):
        return lax.dynamic_index_in_dim(part, jnp.clip(d, 0, n - 1), 0, keepdims=False)

    def add(a, b):
        return (a.astype(jnp.float32) + b.astype(jnp.float32)).astype(jnp.bfloat16)

    ends = [(0, 1), (n - 1, n - 2)]
    if n > 3:
        sent = [
            lax.ppermute(block(jnp.where(p == 0, n - r, r - 1)), "row", ends) for r in range(1, n)
        ]
        zero = jnp.zeros_like(sent[0])
        origin_up = [jnp.where(p == 1, s, zero) for s in sent]
        origin_down = [jnp.where(p == n - 2, s, zero) for s in sent]
    else:
        origin_up = [lax.ppermute(part[n - r], "row", ends[:1]) for r in range(1, n)]
        origin_down = [lax.ppermute(part[r - 1], "row", ends[1:]) for r in range(1, n)]
    with jax.named_scope("up"):
        plus = origin_up[0]
        for r in range(2, n):
            sent = lax.ppermute(add(block(p + n - r), plus), "row", [(q, q + 1) for q in range(1, r)])
            plus = origin_up[r - 1] + sent
    with jax.named_scope("down"):
        minus = origin_down[0]
        for r in range(2, n):
            sent = lax.ppermute(add(block(p - n + r), minus), "row", [(q, q - 1) for q in range(n - r, n - 1)])
            minus = origin_down[r - 1] + sent
    return plus, minus, (origin_up[0], origin_down[0])


def on_device(tokens, gate_up, n, m):
    p = lax.axis_index("row")
    gathered = gather_cols(tokens, m)
    t = gathered.shape[0]
    tb = t // n
    f = gate_up.shape[2]
    units = f // 128
    k = min(CHUNKS, units)
    edges = [128 * (units * i // k) for i in range(k + 1)]
    edges[-1] = f
    outs = []
    held = gathered
    for i in range(k):
        w = gate_up[:, :, edges[i] : edges[i + 1]]
        part = jnp.einsum("td,gdf->tgf", held, w, preferred_element_type=jnp.float32).astype(jnp.bfloat16)
        part = part.reshape(n, tb, 2, edges[i + 1] - edges[i])
        own = lax.dynamic_index_in_dim(part, p, 0, keepdims=False).astype(jnp.float32)
        if n > 1:
            plus, minus, first = line_reduce(part, n, p)
            held = lax.optimization_barrier((gathered, first))[0]
            own = own + plus.astype(jnp.float32) + minus.astype(jnp.float32)
        outs.append((jax.nn.silu(own[:, 0]) * own[:, 1]).astype(jnp.bfloat16))
    return jnp.concatenate(outs, axis=1)


def solution(mesh):
    n = mesh.shape["row"]
    m = mesh.shape["col"]
    placed = (P(("grp", "col"), "row"), P(None, "row", "col"))

    def body(tokens, gate_up):
        return on_device(tokens, gate_up, n, m)

    return jax.shard_map(
        body, mesh=mesh, in_specs=placed, out_specs=P(("grp", "row"), "col"), check_vma=False
    )
```

```python
import jax
import jax.numpy as jnp
from jax import lax
from jax.sharding import PartitionSpec as P

CHUNKS = 2


def gather_cols(tokens, m):
    c = lax.axis_index("col")
    rows = tokens.shape[0]
    buf = jnp.zeros((m, rows, tokens.shape[1]), tokens.dtype)
    buf = lax.dynamic_update_index_in_dim(buf, tokens, c, 0)
    for s in range(1, m):
        got = lax.ppermute(tokens, "col", [(i, (i + s) % m) for i in range(m)])
        buf = lax.dynamic_update_index_in_dim(buf, got, (c - s + m) % m, 0)
    return buf.reshape(m * rows, tokens.shape[1])


def line_reduce(part, n, p):
    def block(d):
        return lax.dynamic_index_in_dim(part, jnp.clip(d, 0, n - 1), 0, keepdims=False)

    def add(a, b):
        return (a.astype(jnp.float32) + b.astype(jnp.float32)).astype(jnp.bfloat16)

    with jax.named_scope("up"):
        origin = [lax.ppermute(part[n - r], "row", [(0, 1)]) for r in range(1, n)]
        plus = origin[0]
        first = plus
        for r in range(2, n):
            sent = lax.ppermute(add(block(p + n - r), plus), "row", [(q, q + 1) for q in range(1, r)])
            plus = origin[r - 1] + sent
            if r == 2:
                first = sent
    with jax.named_scope("down"):
        origin = [lax.ppermute(part[r - 1], "row", [(n - 1, n - 2)]) for r in range(1, n)]
        minus = origin[0]
        second = minus
        for r in range(2, n):
            sent = lax.ppermute(add(block(p - n + r), minus), "row", [(q, q - 1) for q in range(n - r, n - 1)])
            minus = origin[r - 1] + sent
            if r == 2:
                second = sent
    return plus, minus, (first, second)


def on_device(tokens, gate_up, n, m):
    p = lax.axis_index("row")
    gathered = gather_cols(tokens, m)
    t = gathered.shape[0]
    tb = t // n
    f = gate_up.shape[2]
    units = f // 128
    k = min(CHUNKS, units)
    edges = [128 * (units * i // k) for i in range(k + 1)]
    edges[-1] = f
    outs = []
    held = gathered
    for i in range(k):
        w = gate_up[:, :, edges[i] : edges[i + 1]]
        part = jnp.einsum("td,gdf->tgf", held, w, preferred_element_type=jnp.float32).astype(jnp.bfloat16)
        part = part.reshape(n, tb, 2, edges[i + 1] - edges[i])
        own = lax.dynamic_index_in_dim(part, p, 0, keepdims=False).astype(jnp.float32)
        if n > 1:
            plus, minus, first = line_reduce(part, n, p)
            held = lax.optimization_barrier((gathered, first))[0]
            own = own + plus.astype(jnp.float32) + minus.astype(jnp.float32)
        outs.append((jax.nn.silu(own[:, 0]) * own[:, 1]).astype(jnp.bfloat16))
    return jnp.concatenate(outs, axis=1)


def solution(mesh):
    n = mesh.shape["row"]
    m = mesh.shape["col"]
    placed = (P(("grp", "col"), "row"), P(None, "row", "col"))

    def body(tokens, gate_up):
        return on_device(tokens, gate_up, n, m)

    return jax.shard_map(
        body, mesh=mesh, in_specs=placed, out_specs=P(("grp", "row"), "col"), check_vma=False
    )
```

```python
import math

import jax
import jax.numpy as jnp
from jax import lax
from jax.experimental import pallas as pl
from jax.experimental.pallas import tpu as pltpu
from jax.sharding import PartitionSpec as P

CHUNKS = 2


def gather_cols(tokens, m):
    c = lax.axis_index("col")
    rows = tokens.shape[0]
    buf = jnp.zeros((m, rows, tokens.shape[1]), tokens.dtype)
    buf = lax.dynamic_update_index_in_dim(buf, tokens, c, 0)
    for s in range(1, m):
        got = lax.ppermute(tokens, "col", [(i, (i + s) % m) for i in range(m)])
        buf = lax.dynamic_update_index_in_dim(buf, got, (c - s + m) % m, 0)
    return buf.reshape(m * rows, tokens.shape[1])


def tile_width(lo, width, depth):
    step = 128
    units = width // step
    common = units if lo == 0 else math.gcd(lo // step, units)
    best = 1
    for g in range(1, common + 1):
        if common % g == 0 and depth * step * g * 2 <= 9 * 2**20:
            best = g
    return step * best


def project(x, w, lo, width):
    t, d = x.shape
    tf = tile_width(lo, width, d)
    base = lo // tf

    def kernel(x_ref, w_ref, o_ref):
        o_ref[0] = jnp.dot(x_ref[...], w_ref[0], preferred_element_type=jnp.float32).astype(o_ref.dtype)

    return pl.pallas_call(
        kernel,
        out_shape=jax.ShapeDtypeStruct((2, t, width), x.dtype),
        grid=(2, width // tf),
        in_specs=[
            pl.BlockSpec((t, d), lambda g, j: (0, 0)),
            pl.BlockSpec((1, d, tf), lambda g, j: (g, 0, base + j)),
        ],
        out_specs=pl.BlockSpec((1, t, tf), lambda g, j: (g, 0, j)),
        compiler_params=pltpu.CompilerParams(vmem_limit_bytes=48 * 2**20),
        cost_estimate=pl.CostEstimate(
            flops=4 * t * d * width, bytes_accessed=4 * d * width + 2 * t * d + 4 * t * width, transcendentals=0
        ),
    )(x, w)


def line_reduce(part, n, p):
    def block(d):
        return lax.dynamic_index_in_dim(part, jnp.clip(d, 0, n - 1), 1, keepdims=False)

    def add(a, b):
        return (a.astype(jnp.float32) + b.astype(jnp.float32)).astype(jnp.bfloat16)

    with jax.named_scope("up"):
        origin = [lax.ppermute(part[:, n - r], "row", [(0, 1)]) for r in range(1, n)]
        first = origin[0]
        plus = origin[0]
        for r in range(2, n):
            sent = lax.ppermute(add(block(p + n - r), plus), "row", [(q, q + 1) for q in range(1, r)])
            plus = origin[r - 1] + sent
    with jax.named_scope("down"):
        origin = [lax.ppermute(part[:, r - 1], "row", [(n - 1, n - 2)]) for r in range(1, n)]
        minus = origin[0]
        for r in range(2, n):
            sent = lax.ppermute(add(block(p - n + r), minus), "row", [(q, q - 1) for q in range(n - r, n - 1)])
            minus = origin[r - 1] + sent
    return plus, minus, (first, origin[0])


def on_device(tokens, gate_up, n, m):
    p = lax.axis_index("row")
    gathered = gather_cols(tokens, m)
    t = gathered.shape[0]
    tb = t // n
    f = gate_up.shape[2]
    units = f // 128
    k = min(CHUNKS, units)
    edges = [128 * (units * i // k) for i in range(k + 1)]
    edges[-1] = f
    outs = []
    held = gathered
    for i in range(k):
        part = project(held, gate_up, edges[i], edges[i + 1] - edges[i])
        part = part.reshape(2, n, tb, edges[i + 1] - edges[i])
        own = lax.dynamic_index_in_dim(part, p, 1, keepdims=False).astype(jnp.float32)
        if n > 1:
            plus, minus, first = line_reduce(part, n, p)
            held = lax.optimization_barrier((gathered, first))[0]
            own = own + plus.astype(jnp.float32) + minus.astype(jnp.float32)
        outs.append((jax.nn.silu(own[0]) * own[1]).astype(jnp.bfloat16))
    return jnp.concatenate(outs, axis=1)


def solution(mesh):
    n = mesh.shape["row"]
    m = mesh.shape["col"]
    placed = (P(("grp", "col"), "row"), P(None, "row", "col"))

    def body(tokens, gate_up):
        return on_device(tokens, gate_up, n, m)

    return jax.shard_map(
        body, mesh=mesh, in_specs=placed, out_specs=P(("grp", "row"), "col"), check_vma=False
    )
```

```python
import math

import jax
import jax.numpy as jnp
from jax import lax
from jax.experimental import pallas as pl
from jax.experimental.pallas import tpu as pltpu
from jax.sharding import PartitionSpec as P


CHUNKS = 2


def gather_cols(tokens, m):
    c = lax.axis_index("col")
    rows = tokens.shape[0]
    buf = jnp.zeros((m, rows, tokens.shape[1]), tokens.dtype)
    buf = lax.dynamic_update_index_in_dim(buf, tokens, c, 0)
    for s in range(1, m):
        got = lax.ppermute(tokens, "col", [(i, (i + s) % m) for i in range(m)])
        buf = lax.dynamic_update_index_in_dim(buf, got, (c - s + m) % m, 0)
    return buf.reshape(m * rows, tokens.shape[1])


def tile_width(lo, width, depth):
    step = 128
    units = width // step
    common = units if lo == 0 else math.gcd(lo // step, units)
    best = 1
    for g in range(1, common + 1):
        if common % g == 0 and depth * step * g * 2 <= 9 * 2**20:
            best = g
    return step * best


def project(x, w, lo, width):
    t, d = x.shape
    tf = tile_width(lo, width, d)
    base = lo // tf

    def kernel(x_ref, w_ref, o_ref):
        o_ref[0] = jnp.dot(x_ref[...], w_ref[0], preferred_element_type=jnp.float32).astype(o_ref.dtype)

    return pl.pallas_call(
        kernel,
        out_shape=jax.ShapeDtypeStruct((2, t, width), x.dtype),
        grid=(2, width // tf),
        in_specs=[
            pl.BlockSpec((t, d), lambda g, j: (0, 0)),
            pl.BlockSpec((1, d, tf), lambda g, j: (g, 0, base + j)),
        ],
        out_specs=pl.BlockSpec((1, t, tf), lambda g, j: (g, 0, j)),
        compiler_params=pltpu.CompilerParams(vmem_limit_bytes=48 * 2**20),
        cost_estimate=pl.CostEstimate(
            flops=4 * t * d * width, bytes_accessed=4 * d * width + 2 * t * d + 4 * t * width, transcendentals=0
        ),
    )(x, w)


def line_reduce(part, n, p):
    down = lax.optimization_barrier(part)

    def block(d, src=part):
        return lax.dynamic_index_in_dim(src, jnp.clip(d, 0, n - 1), 1, keepdims=False)

    def add(a, b):
        return (a.astype(jnp.float32) + b.astype(jnp.float32)).astype(jnp.bfloat16)

    origin = []
    for r in range(1, n):
        origin.append(lax.ppermute(part[:, n - r], "row", [(0, 1)]))
    first = origin[0]
    plus = origin[0]
    for r in range(2, n):
        sent = lax.ppermute(add(block(p + n - r), plus), "row", [(q, q + 1) for q in range(1, r)])
        plus = origin[r - 1] + sent
    origin = []
    for r in range(1, n):
        origin.append(lax.ppermute(down[:, r - 1], "row", [(n - 1, n - 2)]))
    minus = origin[0]
    for r in range(2, n):
        sent = lax.ppermute(add(block(p - n + r, down), minus), "row", [(q, q - 1) for q in range(n - r, n - 1)])
        minus = origin[r - 1] + sent
    return plus, minus, (first, origin[0])


def on_device(tokens, gate_up, n, m):
    p = lax.axis_index("row")
    gathered = gather_cols(tokens, m)
    t = gathered.shape[0]
    tb = t // n
    f = gate_up.shape[2]
    units = f // 128
    k = min(CHUNKS, units)
    edges = [128 * (units * i // k) for i in range(k + 1)]
    edges[-1] = f
    outs = []
    held = gathered
    for i in range(k):
        part = project(held, gate_up, edges[i], edges[i + 1] - edges[i])
        part = part.reshape(2, n, tb, edges[i + 1] - edges[i])
        own = lax.dynamic_index_in_dim(part, p, 1, keepdims=False).astype(jnp.float32)
        if n > 1:
            plus, minus, first = line_reduce(part, n, p)
            held = lax.optimization_barrier((gathered, first))[0]
            own = own + plus.astype(jnp.float32) + minus.astype(jnp.float32)
        outs.append((jax.nn.silu(own[0]) * own[1]).astype(jnp.bfloat16))
    return jnp.concatenate(outs, axis=1)


def solution(mesh):
    n = mesh.shape["row"]
    m = mesh.shape["col"]
    placed = (P(("grp", "col"), "row"), P(None, "row", "col"))

    def body(tokens, gate_up):
        return on_device(tokens, gate_up, n, m)

    return jax.shard_map(
        body, mesh=mesh, in_specs=placed, out_specs=P(("grp", "row"), "col"), check_vma=False
    )
```

```python
import jax
import jax.numpy as jnp
from jax import lax
from jax.sharding import PartitionSpec as P

CHUNKS = 2


def gather_cols(tokens, m):
    c = lax.axis_index("col")
    rows = tokens.shape[0]
    buf = jnp.zeros((m, rows, tokens.shape[1]), tokens.dtype)
    buf = lax.dynamic_update_index_in_dim(buf, tokens, c, 0)
    for s in range(1, m):
        got = lax.ppermute(tokens, "col", [(i, (i + s) % m) for i in range(m)])
        buf = lax.dynamic_update_index_in_dim(buf, got, (c - s + m) % m, 0)
    return buf.reshape(m * rows, tokens.shape[1])


def line_reduce(part, n, p):
    def block(d):
        return lax.dynamic_index_in_dim(part, jnp.clip(d, 0, n - 1), 0, keepdims=False)

    def add(a, b):
        return (a.astype(jnp.float32) + b.astype(jnp.float32)).astype(jnp.bfloat16)

    with jax.named_scope("up"):
        origin = [lax.ppermute(part[n - r], "row", [(0, 1)]) for r in range(1, n)]
        first = origin[0]
        plus = origin[0]
        for r in range(2, n):
            sent = lax.ppermute(add(block(p + n - r), plus), "row", [(q, q + 1) for q in range(1, r)])
            plus = origin[r - 1] + sent
    with jax.named_scope("down"):
        origin = [lax.ppermute(part[r - 1], "row", [(n - 1, n - 2)]) for r in range(1, n)]
        minus = origin[0]
        for r in range(2, n):
            sent = lax.ppermute(add(block(p - n + r), minus), "row", [(q, q - 1) for q in range(n - r, n - 1)])
            minus = origin[r - 1] + sent
    return plus, minus, (first, origin[0])


def on_device(tokens, gate_up, n, m):
    p = lax.axis_index("row")
    gathered = lax.all_gather(tokens, "col", axis=0, tiled=True)
    t = gathered.shape[0]
    tb = t // n
    f = gate_up.shape[2]
    units = f // 128
    k = min(CHUNKS, units)
    edges = [128 * (units * i // k) for i in range(k + 1)]
    edges[-1] = f
    outs = []
    held = gathered
    for i in range(k):
        w = gate_up[:, :, edges[i] : edges[i + 1]]
        part = jnp.einsum("td,gdf->tgf", held, w, preferred_element_type=jnp.float32).astype(jnp.bfloat16)
        part = part.reshape(n, tb, 2, edges[i + 1] - edges[i])
        own = lax.dynamic_index_in_dim(part, p, 0, keepdims=False).astype(jnp.float32)
        if n > 1:
            plus, minus, first = line_reduce(part, n, p)
            held = lax.optimization_barrier((gathered, first))[0]
            own = own + plus.astype(jnp.float32) + minus.astype(jnp.float32)
        outs.append((jax.nn.silu(own[:, 0]) * own[:, 1]).astype(jnp.bfloat16))
    return jnp.concatenate(outs, axis=1)


def solution(mesh):
    n = mesh.shape["row"]
    m = mesh.shape["col"]
    placed = (P(("grp", "col"), "row"), P(None, "row", "col"))

    def body(tokens, gate_up):
        return on_device(tokens, gate_up, n, m)

    return jax.shard_map(
        body, mesh=mesh, in_specs=placed, out_specs=P(("grp", "row"), "col"), check_vma=False
    )
```

```python
import jax
import jax.numpy as jnp
from jax import lax
from jax.sharding import PartitionSpec as P

CHUNKS = 2


def gather_cols(tokens, m):
    c = lax.axis_index("col")
    rows = tokens.shape[0]
    buf = jnp.zeros((m, rows, tokens.shape[1]), tokens.dtype)
    buf = lax.dynamic_update_index_in_dim(buf, tokens, c, 0)
    for s in range(1, m):
        got = lax.ppermute(tokens, "col", [(i, (i + s) % m) for i in range(m)])
        buf = lax.dynamic_update_index_in_dim(buf, got, (c - s + m) % m, 0)
    return buf.reshape(m * rows, tokens.shape[1])


def line_reduce(part, n, p):
    down = lax.optimization_barrier(part)

    def block(d, src=part):
        return lax.dynamic_index_in_dim(src, jnp.clip(d, 0, n - 1), 0, keepdims=False)

    def add(a, b):
        return (a.astype(jnp.float32) + b.astype(jnp.float32)).astype(jnp.bfloat16)

    with jax.named_scope("up"):
        origin = [lax.ppermute(part[n - r], "row", [(0, 1)]) for r in range(1, n)]
        first = origin[0]
        plus = origin[0]
        for r in range(2, n):
            sent = lax.ppermute(add(block(p + n - r), plus), "row", [(q, q + 1) for q in range(1, r)])
            plus = origin[r - 1] + sent
    with jax.named_scope("down"):
        origin = [lax.ppermute(down[r - 1], "row", [(n - 1, n - 2)]) for r in range(1, n)]
        minus = origin[0]
        for r in range(2, n):
            sent = lax.ppermute(add(block(p - n + r, down), minus), "row", [(q, q - 1) for q in range(n - r, n - 1)])
            minus = origin[r - 1] + sent
    return plus, minus, (first, origin[0])


def on_device(tokens, gate_up, n, m):
    p = lax.axis_index("row")
    gathered = gather_cols(tokens, m)
    t = gathered.shape[0]
    tb = t // n
    f = gate_up.shape[2]
    units = f // 128
    k = min(CHUNKS, units)
    edges = [128 * (units * i // k) for i in range(k + 1)]
    edges[-1] = f
    outs = []
    held = gathered
    for i in range(k):
        w = gate_up[:, :, edges[i] : edges[i + 1]]
        part = jnp.einsum("td,gdf->tgf", held, w, preferred_element_type=jnp.float32).astype(jnp.bfloat16)
        part = part.reshape(n, tb, 2, edges[i + 1] - edges[i])
        own = lax.dynamic_index_in_dim(part, p, 0, keepdims=False).astype(jnp.float32)
        if n > 1:
            plus, minus, first = line_reduce(part, n, p)
            held = lax.optimization_barrier((gathered, first))[0]
            own = own + plus.astype(jnp.float32) + minus.astype(jnp.float32)
        outs.append((jax.nn.silu(own[:, 0]) * own[:, 1]).astype(jnp.bfloat16))
    return jnp.concatenate(outs, axis=1)


def solution(mesh):
    n = mesh.shape["row"]
    m = mesh.shape["col"]
    placed = (P(("grp", "col"), "row"), P(None, "row", "col"))

    def body(tokens, gate_up):
        return on_device(tokens, gate_up, n, m)

    return jax.shard_map(
        body, mesh=mesh, in_specs=placed, out_specs=P(("grp", "row"), "col"), check_vma=False
    )
```

```python
import jax
import jax.numpy as jnp
from jax import lax
from jax.sharding import PartitionSpec as P

SHARES = (2, 1)


def gather_cols(tokens, m):
    c = lax.axis_index("col")
    rows = tokens.shape[0]
    buf = jnp.zeros((m, rows, tokens.shape[1]), tokens.dtype)
    buf = lax.dynamic_update_index_in_dim(buf, tokens, c, 0)
    for s in range(1, m):
        got = lax.ppermute(tokens, "col", [(i, (i + s) % m) for i in range(m)])
        buf = lax.dynamic_update_index_in_dim(buf, got, (c - s + m) % m, 0)
    return buf.reshape(m * rows, tokens.shape[1])


def line_reduce(part, n, p):
    def block(d):
        return lax.dynamic_index_in_dim(part, jnp.clip(d, 0, n - 1), 0, keepdims=False)

    def add(a, b):
        return (a.astype(jnp.float32) + b.astype(jnp.float32)).astype(jnp.bfloat16)

    with jax.named_scope("up"):
        origin = [lax.ppermute(part[n - r], "row", [(0, 1)]) for r in range(1, n)]
        first = origin[0]
        plus = origin[0]
        for r in range(2, n):
            sent = lax.ppermute(add(block(p + n - r), plus), "row", [(q, q + 1) for q in range(1, r)])
            plus = origin[r - 1] + sent
    with jax.named_scope("down"):
        origin = [lax.ppermute(part[r - 1], "row", [(n - 1, n - 2)]) for r in range(1, n)]
        minus = origin[0]
        for r in range(2, n):
            sent = lax.ppermute(add(block(p - n + r), minus), "row", [(q, q - 1) for q in range(n - r, n - 1)])
            minus = origin[r - 1] + sent
    return plus, minus, (first, origin[0])


def on_device(tokens, gate_up, n, m):
    p = lax.axis_index("row")
    gathered = gather_cols(tokens, m)
    t = gathered.shape[0]
    tb = t // n
    f = gate_up.shape[2]
    units = f // 128
    shares = SHARES[: max(1, min(len(SHARES), units))]
    k = len(shares)
    edges = [128 * (units * sum(shares[:i]) // sum(shares)) for i in range(k + 1)]
    edges[-1] = f
    outs = []
    held = gathered
    for i in range(k):
        w = gate_up[:, :, edges[i] : edges[i + 1]]
        part = jnp.einsum("td,gdf->tgf", held, w, preferred_element_type=jnp.float32).astype(jnp.bfloat16)
        part = part.reshape(n, tb, 2, edges[i + 1] - edges[i])
        own = lax.dynamic_index_in_dim(part, p, 0, keepdims=False).astype(jnp.float32)
        if n > 1:
            plus, minus, first = line_reduce(part, n, p)
            held = lax.optimization_barrier((gathered, first))[0]
            own = own + plus.astype(jnp.float32) + minus.astype(jnp.float32)
        outs.append((jax.nn.silu(own[:, 0]) * own[:, 1]).astype(jnp.bfloat16))
    return jnp.concatenate(outs, axis=1)


def solution(mesh):
    n = mesh.shape["row"]
    m = mesh.shape["col"]
    placed = (P(("grp", "col"), "row"), P(None, "row", "col"))

    def body(tokens, gate_up):
        return on_device(tokens, gate_up, n, m)

    return jax.shard_map(
        body, mesh=mesh, in_specs=placed, out_specs=P(("grp", "row"), "col"), check_vma=False
    )
```

```python
import jax
import jax.numpy as jnp
from jax import lax
from jax.sharding import PartitionSpec as P

SHARES = (1, 1, 1)


def gather_cols(tokens, m):
    c = lax.axis_index("col")
    rows = tokens.shape[0]
    buf = jnp.zeros((m, rows, tokens.shape[1]), tokens.dtype)
    buf = lax.dynamic_update_index_in_dim(buf, tokens, c, 0)
    for s in range(1, m):
        got = lax.ppermute(tokens, "col", [(i, (i + s) % m) for i in range(m)])
        buf = lax.dynamic_update_index_in_dim(buf, got, (c - s + m) % m, 0)
    return buf.reshape(m * rows, tokens.shape[1])


def line_reduce(part, n, p):
    def block(d):
        return lax.dynamic_index_in_dim(part, jnp.clip(d, 0, n - 1), 0, keepdims=False)

    def add(a, b):
        return (a.astype(jnp.float32) + b.astype(jnp.float32)).astype(jnp.bfloat16)

    with jax.named_scope("up"):
        origin = [lax.ppermute(part[n - r], "row", [(0, 1)]) for r in range(1, n)]
        first = origin[0]
        plus = origin[0]
        for r in range(2, n):
            sent = lax.ppermute(add(block(p + n - r), plus), "row", [(q, q + 1) for q in range(1, r)])
            plus = origin[r - 1] + sent
    with jax.named_scope("down"):
        origin = [lax.ppermute(part[r - 1], "row", [(n - 1, n - 2)]) for r in range(1, n)]
        minus = origin[0]
        for r in range(2, n):
            sent = lax.ppermute(add(block(p - n + r), minus), "row", [(q, q - 1) for q in range(n - r, n - 1)])
            minus = origin[r - 1] + sent
    return plus, minus, (first, origin[0])


def on_device(tokens, gate_up, n, m):
    p = lax.axis_index("row")
    gathered = gather_cols(tokens, m)
    t = gathered.shape[0]
    tb = t // n
    f = gate_up.shape[2]
    units = f // 128
    shares = SHARES[: max(1, min(len(SHARES), units))]
    k = len(shares)
    edges = [128 * (units * sum(shares[:i]) // sum(shares)) for i in range(k + 1)]
    edges[-1] = f
    outs = []
    held = gathered
    for i in range(k):
        w = gate_up[:, :, edges[i] : edges[i + 1]]
        part = jnp.einsum("td,gdf->tgf", held, w, preferred_element_type=jnp.float32).astype(jnp.bfloat16)
        part = part.reshape(n, tb, 2, edges[i + 1] - edges[i])
        own = lax.dynamic_index_in_dim(part, p, 0, keepdims=False).astype(jnp.float32)
        if n > 1:
            plus, minus, first = line_reduce(part, n, p)
            held = lax.optimization_barrier((gathered, first))[0]
            own = own + plus.astype(jnp.float32) + minus.astype(jnp.float32)
        outs.append((jax.nn.silu(own[:, 0]) * own[:, 1]).astype(jnp.bfloat16))
    return jnp.concatenate(outs, axis=1)


def solution(mesh):
    n = mesh.shape["row"]
    m = mesh.shape["col"]
    placed = (P(("grp", "col"), "row"), P(None, "row", "col"))

    def body(tokens, gate_up):
        return on_device(tokens, gate_up, n, m)

    return jax.shard_map(
        body, mesh=mesh, in_specs=placed, out_specs=P(("grp", "row"), "col"), check_vma=False
    )
```

```python
import math

import jax
import jax.numpy as jnp
from jax import lax
from jax.experimental import pallas as pl
from jax.experimental.pallas import tpu as pltpu
from jax.sharding import PartitionSpec as P


CHUNKS = 2


def tile_width(lo, width, depth):
    step = 128
    units = width // step
    common = units if lo == 0 else math.gcd(lo // step, units)
    best = 1
    for g in range(1, common + 1):
        if common % g == 0 and depth * step * g * 2 <= 9 * 2**20:
            best = g
    return step * best


def project(x, w, lo, width):
    t, d = x.shape
    tf = tile_width(lo, width, d)
    base = lo // tf

    def kernel(x_ref, w_ref, o_ref):
        o_ref[0] = jnp.dot(x_ref[...], w_ref[0], preferred_element_type=jnp.float32).astype(o_ref.dtype)

    return pl.pallas_call(
        kernel,
        out_shape=jax.ShapeDtypeStruct((2, t, width), x.dtype),
        grid=(2, width // tf),
        in_specs=[
            pl.BlockSpec((t, d), lambda g, j: (0, 0)),
            pl.BlockSpec((1, d, tf), lambda g, j: (g, 0, base + j)),
        ],
        out_specs=pl.BlockSpec((1, t, tf), lambda g, j: (g, 0, j)),
        compiler_params=pltpu.CompilerParams(vmem_limit_bytes=48 * 2**20),
        cost_estimate=pl.CostEstimate(
            flops=4 * t * d * width, bytes_accessed=4 * d * width + 2 * t * d + 4 * t * width, transcendentals=0
        ),
    )(x, w)


def line_reduce(part, n, p):
    def block(d):
        return lax.dynamic_index_in_dim(part, jnp.clip(d, 0, n - 1), 1, keepdims=False)

    def add(a, b):
        return (a.astype(jnp.float32) + b.astype(jnp.float32)).astype(jnp.bfloat16)

    origin = []
    for r in range(1, n):
        origin.append(lax.ppermute(part[:, n - r], "row", [(0, 1)]))
    first = origin[0]
    plus = origin[0]
    for r in range(2, n):
        sent = lax.ppermute(add(block(p + n - r), plus), "row", [(q, q + 1) for q in range(1, r)])
        plus = origin[r - 1] + sent
    origin = []
    for r in range(1, n):
        origin.append(lax.ppermute(part[:, r - 1], "row", [(n - 1, n - 2)]))
    minus = origin[0]
    for r in range(2, n):
        sent = lax.ppermute(add(block(p - n + r), minus), "row", [(q, q - 1) for q in range(n - r, n - 1)])
        minus = origin[r - 1] + sent
    return plus, minus, (first, origin[0])


def on_device(tokens, gate_up, n):
    p = lax.axis_index("row")
    gathered = lax.all_gather(tokens, "col", axis=0, tiled=True)
    t = gathered.shape[0]
    tb = t // n
    f = gate_up.shape[2]
    units = f // 128
    k = min(CHUNKS, units)
    edges = [128 * (units * i // k) for i in range(k + 1)]
    edges[-1] = f
    outs = []
    held = gathered
    for i in range(k):
        part = project(held, gate_up, edges[i], edges[i + 1] - edges[i])
        part = part.reshape(2, n, tb, edges[i + 1] - edges[i])
        own = lax.dynamic_index_in_dim(part, p, 1, keepdims=False).astype(jnp.float32)
        if n > 1:
            plus, minus, first = line_reduce(part, n, p)
            held = lax.optimization_barrier((gathered, first))[0]
            own = own + plus.astype(jnp.float32) + minus.astype(jnp.float32)
        outs.append((jax.nn.silu(own[0]) * own[1]).astype(jnp.bfloat16))
    return jnp.concatenate(outs, axis=1)


def solution(mesh):
    n = mesh.shape["row"]
    placed = (P(("grp", "col"), "row"), P(None, "row", "col"))

    def body(tokens, gate_up):
        return on_device(tokens, gate_up, n)

    return jax.shard_map(
        body, mesh=mesh, in_specs=placed, out_specs=P(("grp", "row"), "col"), check_vma=False
    )
```

```python
import jax
import jax.numpy as jnp
from jax import lax
from jax.sharding import PartitionSpec as P


CHUNKS = 2


def gather_cols(tokens, m):
    c = lax.axis_index("col")
    rows = tokens.shape[0]
    buf = jnp.zeros((m, rows, tokens.shape[1]), tokens.dtype)
    buf = lax.dynamic_update_index_in_dim(buf, tokens, c, 0)
    for s in range(1, m):
        got = lax.ppermute(tokens, "col", [(i, (i + s) % m) for i in range(m)])
        buf = lax.dynamic_update_index_in_dim(buf, got, (c - s + m) % m, 0)
    return buf.reshape(m * rows, tokens.shape[1])


def line_reduce(part, n, p):
    def block(d):
        return lax.dynamic_index_in_dim(part, jnp.clip(d, 0, n - 1), 0, keepdims=False)

    def add(a, b):
        return (a.astype(jnp.float32) + b.astype(jnp.float32)).astype(jnp.bfloat16)

    origin = []
    for r in range(1, n):
        origin.append(lax.ppermute(part[n - r], "row", [(0, 1)]))
    first = origin[0]
    plus = origin[0]
    for r in range(2, n):
        sent = lax.ppermute(add(block(p + n - r), plus), "row", [(q, q + 1) for q in range(1, r)])
        plus = origin[r - 1] + sent
    origin = []
    for r in range(1, n):
        origin.append(lax.ppermute(part[r - 1], "row", [(n - 1, n - 2)]))
    minus = origin[0]
    for r in range(2, n):
        sent = lax.ppermute(add(block(p - n + r), minus), "row", [(q, q - 1) for q in range(n - r, n - 1)])
        minus = origin[r - 1] + sent
    return plus, minus, (first, origin[0])


def on_device(tokens, gate_up, n, m):
    p = lax.axis_index("row")
    gathered = gather_cols(tokens, m)
    t = gathered.shape[0]
    tb = t // n
    f = gate_up.shape[2]
    units = f // 128
    k = min(CHUNKS, units)
    edges = [128 * (units * i // k) for i in range(k + 1)]
    edges[-1] = f
    outs = []
    for i in range(k):
        w = gate_up[:, :, edges[i] : edges[i + 1]]
        part = jnp.einsum("td,gdf->tgf", gathered, w, preferred_element_type=jnp.float32).astype(jnp.bfloat16)
        part = part.reshape(n, tb, 2, edges[i + 1] - edges[i])
        own = lax.dynamic_index_in_dim(part, p, 0, keepdims=False).astype(jnp.float32)
        if n > 1:
            plus, minus, _ = line_reduce(part, n, p)
            own = own + plus.astype(jnp.float32) + minus.astype(jnp.float32)
        outs.append((jax.nn.silu(own[:, 0]) * own[:, 1]).astype(jnp.bfloat16))
    return jnp.concatenate(outs, axis=1)


def solution(mesh):
    n = mesh.shape["row"]
    m = mesh.shape["col"]
    placed = (P(("grp", "col"), "row"), P(None, "row", "col"))

    def body(tokens, gate_up):
        return on_device(tokens, gate_up, n, m)

    return jax.shard_map(
        body, mesh=mesh, in_specs=placed, out_specs=P(("grp", "row"), "col"), check_vma=False
    )
```

```python
import jax
import jax.numpy as jnp
from jax import lax
from jax.sharding import PartitionSpec as P

CHUNKS = 2


def gather_cols(tokens, m):
    c = lax.axis_index("col")
    rows = tokens.shape[0]
    buf = jnp.zeros((m, rows, tokens.shape[1]), tokens.dtype)
    buf = lax.dynamic_update_index_in_dim(buf, tokens, c, 0)
    for s in range(1, m):
        got = lax.ppermute(tokens, "col", [(i, (i + s) % m) for i in range(m)])
        buf = lax.dynamic_update_index_in_dim(buf, got, (c - s + m) % m, 0)
    return buf.reshape(m * rows, tokens.shape[1])


def line_reduce(part, n, p):
    def block(d):
        return lax.dynamic_index_in_dim(part, jnp.clip(d, 0, n - 1), 0, keepdims=False)

    def add(a, b):
        return (a.astype(jnp.float32) + b.astype(jnp.float32)).astype(jnp.bfloat16)

    with jax.named_scope("up"):
        origin = [lax.ppermute(part[n - r], "row", [(0, 1)]) for r in range(1, n)]
        first = origin[0]
        plus = origin[0]
        for r in range(2, n):
            sent = lax.ppermute(add(block(p + n - r), plus), "row", [(q, q + 1) for q in range(1, r)])
            plus = origin[r - 1] + sent
    with jax.named_scope("down"):
        origin = [lax.ppermute(part[r - 1], "row", [(n - 1, n - 2)]) for r in range(1, n)]
        minus = origin[0]
        for r in range(2, n):
            sent = lax.ppermute(add(block(p - n + r), minus), "row", [(q, q - 1) for q in range(n - r, n - 1)])
            minus = origin[r - 1] + sent
    return plus, minus, (first, origin[0])


def on_device(tokens, gate_up, n, m):
    p = lax.axis_index("row")
    gathered = gather_cols(tokens, m)
    t = gathered.shape[0]
    tb = t // n
    f = gate_up.shape[2]
    units = f // 128
    k = min(CHUNKS, units)
    edges = [128 * (units * i // k) for i in range(k + 1)]
    edges[-1] = f
    outs = []
    held = gathered
    for i in range(k):
        w = gate_up[:, :, edges[i] : edges[i + 1]]
        part = jnp.einsum("td,gdf->tgf", held, w, preferred_element_type=jnp.float32).astype(jnp.bfloat16)
        if i == k - 1 and k > 1:
            own = lax.psum_scatter(part, "row", scatter_dimension=0, tiled=True).astype(jnp.float32)
            outs.append((jax.nn.silu(own[:, 0]) * own[:, 1]).astype(jnp.bfloat16))
            continue
        part = part.reshape(n, tb, 2, edges[i + 1] - edges[i])
        own = lax.dynamic_index_in_dim(part, p, 0, keepdims=False).astype(jnp.float32)
        if n > 1:
            plus, minus, first = line_reduce(part, n, p)
            held = lax.optimization_barrier((gathered, first))[0]
            own = own + plus.astype(jnp.float32) + minus.astype(jnp.float32)
        outs.append((jax.nn.silu(own[:, 0]) * own[:, 1]).astype(jnp.bfloat16))
    return jnp.concatenate(outs, axis=1)


def solution(mesh):
    n = mesh.shape["row"]
    m = mesh.shape["col"]
    placed = (P(("grp", "col"), "row"), P(None, "row", "col"))

    def body(tokens, gate_up):
        return on_device(tokens, gate_up, n, m)

    return jax.shard_map(
        body, mesh=mesh, in_specs=placed, out_specs=P(("grp", "row"), "col"), check_vma=False
    )
```

```python
import jax
import jax.numpy as jnp
from jax import lax
from jax.sharding import PartitionSpec as P

CHUNKS = 2


def gather_cols(tokens, m):
    c = lax.axis_index("col")
    rows = tokens.shape[0]
    buf = jnp.zeros((m, rows, tokens.shape[1]), tokens.dtype)
    if m % 2:
        buf = lax.dynamic_update_index_in_dim(buf, tokens, c, 0)
        for s in range(1, m):
            got = lax.ppermute(tokens, "col", [(i, (i + s) % m) for i in range(m)])
            buf = lax.dynamic_update_index_in_dim(buf, got, (c - s + m) % m, 0)
        return buf.reshape(m * rows, tokens.shape[1])
    mine = [tokens] + [
        lax.ppermute(tokens, "col", [(i, (i + 2 * s) % m) for i in range(m)]) for s in range(1, m // 2)
    ]
    other = lax.ppermute(jnp.stack(mine), "col", [(i, i + 1 - 2 * (i % 2)) for i in range(m)])
    partner = c + 1 - 2 * (c % 2)
    for s in range(m // 2):
        buf = lax.dynamic_update_index_in_dim(buf, mine[s], (c - 2 * s + m) % m, 0)
        buf = lax.dynamic_update_index_in_dim(buf, other[s], (partner - 2 * s + m) % m, 0)
    return buf.reshape(m * rows, tokens.shape[1])


def line_reduce(part, n, p):
    def block(d):
        return lax.dynamic_index_in_dim(part, jnp.clip(d, 0, n - 1), 0, keepdims=False)

    def add(a, b):
        return (a.astype(jnp.float32) + b.astype(jnp.float32)).astype(jnp.bfloat16)

    with jax.named_scope("up"):
        origin = [lax.ppermute(part[n - r], "row", [(0, 1)]) for r in range(1, n)]
        first = origin[0]
        plus = origin[0]
        for r in range(2, n):
            sent = lax.ppermute(add(block(p + n - r), plus), "row", [(q, q + 1) for q in range(1, r)])
            plus = origin[r - 1] + sent
    with jax.named_scope("down"):
        origin = [lax.ppermute(part[r - 1], "row", [(n - 1, n - 2)]) for r in range(1, n)]
        minus = origin[0]
        for r in range(2, n):
            sent = lax.ppermute(add(block(p - n + r), minus), "row", [(q, q - 1) for q in range(n - r, n - 1)])
            minus = origin[r - 1] + sent
    return plus, minus, (first, origin[0])


def on_device(tokens, gate_up, n, m):
    p = lax.axis_index("row")
    gathered = gather_cols(tokens, m)
    t = gathered.shape[0]
    tb = t // n
    f = gate_up.shape[2]
    units = f // 128
    k = min(CHUNKS, units)
    edges = [128 * (units * i // k) for i in range(k + 1)]
    edges[-1] = f
    outs = []
    held = gathered
    for i in range(k):
        w = gate_up[:, :, edges[i] : edges[i + 1]]
        part = jnp.einsum("td,gdf->tgf", held, w, preferred_element_type=jnp.float32).astype(jnp.bfloat16)
        part = part.reshape(n, tb, 2, edges[i + 1] - edges[i])
        own = lax.dynamic_index_in_dim(part, p, 0, keepdims=False).astype(jnp.float32)
        if n > 1:
            plus, minus, first = line_reduce(part, n, p)
            held = lax.optimization_barrier((gathered, first))[0]
            own = own + plus.astype(jnp.float32) + minus.astype(jnp.float32)
        outs.append((jax.nn.silu(own[:, 0]) * own[:, 1]).astype(jnp.bfloat16))
    return jnp.concatenate(outs, axis=1)


def solution(mesh):
    n = mesh.shape["row"]
    m = mesh.shape["col"]
    placed = (P(("grp", "col"), "row"), P(None, "row", "col"))

    def body(tokens, gate_up):
        return on_device(tokens, gate_up, n, m)

    return jax.shard_map(
        body, mesh=mesh, in_specs=placed, out_specs=P(("grp", "row"), "col"), check_vma=False
    )
```

```python
import jax
import jax.numpy as jnp
from jax import lax
from jax.sharding import PartitionSpec as P

CHUNKS = 2


def gather_cols(tokens, m):
    c = lax.axis_index("col")
    rows = tokens.shape[0]
    buf = jnp.zeros((m, rows, tokens.shape[1]), tokens.dtype)
    buf = lax.dynamic_update_index_in_dim(buf, tokens, c, 0)
    for s in range(1, m):
        got = lax.ppermute(tokens, "col", [(i, (i + s) % m) for i in range(m)])
        buf = lax.dynamic_update_index_in_dim(buf, got, (c - s + m) % m, 0)
    return buf.reshape(m * rows, tokens.shape[1])


def line_reduce(part, n, p):
    def block(d):
        return lax.dynamic_index_in_dim(part, jnp.clip(d, 0, n - 1), 0, keepdims=False)

    def add(a, b):
        return (a.astype(jnp.float32) + b.astype(jnp.float32)).astype(jnp.bfloat16)

    with jax.named_scope("up"):
        origin = [lax.ppermute(part[n - r], "row", [(0, 1)]) for r in range(1, n)]
        first = origin[0]
        plus = origin[0]
        for r in range(2, n):
            sent = lax.ppermute(add(block(p + n - r), plus), "row", [(q, q + 1) for q in range(1, r)])
            plus = origin[r - 1] + sent
    with jax.named_scope("down"):
        origin = [lax.ppermute(part[r - 1], "row", [(n - 1, n - 2)]) for r in range(1, n)]
        minus = origin[0]
        for r in range(2, n):
            sent = lax.ppermute(add(block(p - n + r), minus), "row", [(q, q - 1) for q in range(n - r, n - 1)])
            minus = origin[r - 1] + sent
    return plus, minus, first


def on_device(tokens, gate_up, n, m):
    p = lax.axis_index("row")
    gathered = gather_cols(tokens, m)
    t = gathered.shape[0]
    tb = t // n
    f = gate_up.shape[2]
    units = f // 128
    k = min(CHUNKS, units)
    edges = [128 * (units * i // k) for i in range(k + 1)]
    edges[-1] = f
    outs = []
    held = gathered
    for i in range(k):
        w = gate_up[:, :, edges[i] : edges[i + 1]]
        part = jnp.einsum("td,gdf->tgf", held, w, preferred_element_type=jnp.float32).astype(jnp.bfloat16)
        part = part.reshape(n, tb, 2, edges[i + 1] - edges[i])
        own = lax.dynamic_index_in_dim(part, p, 0, keepdims=False).astype(jnp.float32)
        if n > 1:
            plus, minus, first = line_reduce(part, n, p)
            held = lax.optimization_barrier((gathered, first))[0]
            own = own + plus.astype(jnp.float32) + minus.astype(jnp.float32)
        outs.append((jax.nn.silu(own[:, 0]) * own[:, 1]).astype(jnp.bfloat16))
    return jnp.concatenate(outs, axis=1)


def solution(mesh):
    n = mesh.shape["row"]
    m = mesh.shape["col"]
    placed = (P(("grp", "col"), "row"), P(None, "row", "col"))

    def body(tokens, gate_up):
        return on_device(tokens, gate_up, n, m)

    return jax.shard_map(
        body, mesh=mesh, in_specs=placed, out_specs=P(("grp", "row"), "col"), check_vma=False
    )
```

```python
import jax
import jax.numpy as jnp
from jax import lax
from jax.sharding import PartitionSpec as P

CHUNKS = 2


def gather_cols(tokens, m):
    c = lax.axis_index("col")
    rows = tokens.shape[0]
    buf = jnp.zeros((m, rows, tokens.shape[1]), tokens.dtype)
    buf = lax.dynamic_update_index_in_dim(buf, tokens, c, 0)
    for s in range(1, m):
        got = lax.ppermute(tokens, "col", [(i, (i + s) % m) for i in range(m)])
        buf = lax.dynamic_update_index_in_dim(buf, got, (c - s + m) % m, 0)
    return buf.reshape(m * rows, tokens.shape[1])


def line_reduce(part, n, p):
    def block(d):
        return lax.dynamic_index_in_dim(part, jnp.clip(d, 0, n - 1), 0, keepdims=False)

    def add(a, b):
        return (a.astype(jnp.float32) + b.astype(jnp.float32)).astype(jnp.bfloat16)

    with jax.named_scope("up"):
        origin = [lax.ppermute(part[n - r], "row", [(0, 1)]) for r in range(1, n)]
        first = origin[0]
        plus = origin[0]
        for r in range(2, n):
            sent = lax.ppermute(add(block(p + n - r), plus), "row", [(q, q + 1) for q in range(1, r)])
            plus = origin[r - 1] + sent
    with jax.named_scope("down"):
        origin = [lax.ppermute(part[r - 1], "row", [(n - 1, n - 2)]) for r in range(1, n)]
        minus = origin[0]
        for r in range(2, n):
            sent = lax.ppermute(add(block(p - n + r), minus), "row", [(q, q - 1) for q in range(n - r, n - 1)])
            minus = origin[r - 1] + sent
    return plus, minus, origin[0]


def on_device(tokens, gate_up, n, m):
    p = lax.axis_index("row")
    gathered = gather_cols(tokens, m)
    t = gathered.shape[0]
    tb = t // n
    f = gate_up.shape[2]
    units = f // 128
    k = min(CHUNKS, units)
    edges = [128 * (units * i // k) for i in range(k + 1)]
    edges[-1] = f
    outs = []
    held = gathered
    for i in range(k):
        w = gate_up[:, :, edges[i] : edges[i + 1]]
        part = jnp.einsum("td,gdf->tgf", held, w, preferred_element_type=jnp.float32).astype(jnp.bfloat16)
        part = part.reshape(n, tb, 2, edges[i + 1] - edges[i])
        own = lax.dynamic_index_in_dim(part, p, 0, keepdims=False).astype(jnp.float32)
        if n > 1:
            plus, minus, first = line_reduce(part, n, p)
            held = lax.optimization_barrier((gathered, first))[0]
            own = own + plus.astype(jnp.float32) + minus.astype(jnp.float32)
        outs.append((jax.nn.silu(own[:, 0]) * own[:, 1]).astype(jnp.bfloat16))
    return jnp.concatenate(outs, axis=1)


def solution(mesh):
    n = mesh.shape["row"]
    m = mesh.shape["col"]
    placed = (P(("grp", "col"), "row"), P(None, "row", "col"))

    def body(tokens, gate_up):
        return on_device(tokens, gate_up, n, m)

    return jax.shard_map(
        body, mesh=mesh, in_specs=placed, out_specs=P(("grp", "row"), "col"), check_vma=False
    )
```
